512 devices in a mesh: ens: 16 (over z, x_hi), tile: 32 (over y, x_lo, core).
Axes of the slice: x: 4 (x_hi: 2, x_lo: 2; x = x_hi * 2 + x_lo), y: 8, z: 8, core: 2. Of those that a mesh axis runs over, the one named last changes fastest.
Arguments:
- conditioning: bfloat16 [12, 256, 128], P(None, 'tile'), may hold values from -6 to 6
- member_noise: float32 [16, 4, 256, 128], P('ens', None, 'tile'), may hold values from -6 to 6
- reg_in: bfloat16 [3, 3, 12, 128], replicated, may hold values from -1 to 1
- reg_down: bfloat16 [3, 3, 128, 128], replicated, may hold values from -0.25 to 0.25
- reg_low: bfloat16 [3, 3, 128, 128], replicated, may hold values from -0.25 to 0.25
- reg_up: bfloat16 [4, 4, 128, 128], replicated, may hold values from -0.375 to 0.375
- reg_fine: bfloat16 [3, 3, 128, 128], replicated, may hold values from -0.25 to 0.25
- reg_out: bfloat16 [3, 3, 4, 128], replicated, may hold values from -0.3125 to 0.3125
- dif_in: bfloat16 [3, 3, 20, 128], replicated, may hold values from -0.75 to 0.75
- dif_down: bfloat16 [3, 3, 128, 128], replicated, may hold values from -0.25 to 0.25
- dif_low: bfloat16 [3, 3, 128, 128], replicated, may hold values from -0.25 to 0.25
- dif_up: bfloat16 [4, 4, 128, 128], replicated, may hold values from -0.375 to 0.375
- dif_fine: bfloat16 [3, 3, 128, 128], replicated, may hold values from -0.25 to 0.25
- dif_out: bfloat16 [3, 3, 4, 128], replicated, may hold values from -0.3125 to 0.3125
Outputs:
- prediction: float32 [16, 4, 256, 128], P('ens', None, 'tile')
The draws below stay inside these ranges and needn't reach their ends.
All inputs are finite; a program needn't handle non-finite values.
Results may differ from the reference program's by a relative error of at most 0.015.
Values may be sent and summed in bfloat16 or wider, within the bound.
No kernel may reach another device: no remote copies, remote signals or barrier semaphores. Data moves between devices by JAX's collectives and lax.ppermute only.
A program may use at most 64 MiB of HBM per device.

```python
import jax
import jax.numpy as jnp
from jax import lax

C = 128
OUTC = 4
CIREG = 12
STEPS = 2
W = 128
CIN = 20
H = 256
ENS = 16


def levels(rng, extent, cuts, low, top_value):
    def one(position, parts):
        heights = jax.random.uniform(jax.random.fold_in(jax.random.fold_in(rng, 6), position), (parts,), jnp.float32, low / len(cuts), top_value / len(cuts))
        return jnp.repeat(jnp.exp(heights), extent[position] // parts).reshape((-1,) + (1,) * (len(extent) - position - 1))

    loudness = one(*cuts[0])
    for cut in cuts[1:]:
        loudness = loudness * one(*cut)
    return loudness


def normal_values(key, shape, scale, bound, cuts=(), kind=jnp.bfloat16):
    result = jax.random.normal(key, shape, jnp.float32) * scale
    if len(cuts) > 0:
        result = levels(key, shape, cuts, -0.22, 0.18) * result
    return jnp.clip(result, min=-bound, max=bound).astype(kind)


def setup_inputs(seed: int = 0) -> dict:
    key_list = jax.random.split(jax.random.key(seed), 15)
    return {
        "conditioning": normal_values(key_list[0], (CIREG, H, W), 1.0, 6.0, ((1, 32),)),
        "member_noise": normal_values(key_list[1], (ENS, OUTC, H, W), 1.0, 6.0, ((0, 16), (2, 32)), jnp.float32),
        "reg_in": normal_values(key_list[2], (3, 3, CIREG, C), (3 * CIREG) ** -0.5, 1.0),
        "reg_down": normal_values(key_list[3], (3, 3, C, C), (4 * C) ** -0.5, 0.25),
        "reg_low": normal_values(key_list[4], (3, 3, C, C), (4 * C) ** -0.5, 0.25),
        "reg_up": normal_values(key_list[5], (4, 4, C, C), (2 * C) ** -0.5, 0.375),
        "reg_fine": normal_values(key_list[6], (3, 3, C, C), (4 * C) ** -0.5, 0.25),
        "reg_out": normal_values(key_list[7], (3, 3, OUTC, C), (3 * C) ** -0.5, 0.3125),
        "dif_in": normal_values(key_list[8], (3, 3, CIN, C), (3 * CIN) ** -0.5, 0.75),
        "dif_down": normal_values(key_list[9], (3, 3, C, C), (4 * C) ** -0.5, 0.25),
        "dif_low": normal_values(key_list[10], (3, 3, C, C), (4 * C) ** -0.5, 0.25),
        "dif_up": normal_values(key_list[11], (4, 4, C, C), (2 * C) ** -0.5, 0.375),
        "dif_fine": normal_values(key_list[12], (3, 3, C, C), (4 * C) ** -0.5, 0.25),
        "dif_out": normal_values(key_list[13], (3, 3, OUTC, C), (3 * C) ** -0.5, 0.3125),
    }


sigma_top = 1.0
sigma_ratio = 0.4
sigma_data = 0.5

def silu_round(values):
    return jax.nn.silu(values).astype(jnp.bfloat16)

def conv_fields(padded, weight):
    height = padded.shape[1] - 2
    across = padded.shape[2] - 2
    running = None
    for tap_y in range(3):
        for tap_x in range(3):
            window = padded[:, tap_y:tap_y + height, tap_x:tap_x + across].astype(jnp.float32)
            tap_term = jnp.einsum('crw,co->rwo', window, weight[tap_y, tap_x].astype(jnp.float32))
            running = tap_term if running is None else running + tap_term
    return running

def conv_feat(padded, weight, stride):
    count_y = (padded.shape[0] - 3) // stride + 1
    count_x = (padded.shape[1] - 3) // stride + 1
    running = None
    for tap_y in range(3):
        for tap_x in range(3):
            window = padded[tap_y:tap_y + stride * (count_y - 1) + 1:stride, tap_x:tap_x + stride * (count_x - 1) + 1:stride]
            tap_term = jnp.einsum('rwc,co->rwo', window.astype(jnp.float32), weight[tap_y, tap_x].astype(jnp.float32))
            running = tap_term if running is None else running + tap_term
    return running

def conv_out(padded, weight):
    height = padded.shape[0] - 2
    across = padded.shape[1] - 2
    running = None
    for tap_y in range(3):
        for tap_x in range(3):
            window = padded[tap_y:tap_y + height, tap_x:tap_x + across].astype(jnp.float32)
            tap_term = jnp.einsum('rwc,oc->orw', window, weight[tap_y, tap_x].astype(jnp.float32))
            running = tap_term if running is None else running + tap_term
    return running

def up_conv(padded, weight):
    count_y = padded.shape[0] - 2
    count_x = padded.shape[1] - 2
    tap_pairs = (((1, 1), (0, 3)), ((2, 0), (1, 2)))

    def parity(side_y, side_x):
        running = None
        for offset_y, kernel_y in tap_pairs[side_y]:
            for offset_x, kernel_x in tap_pairs[side_x]:
                window = padded[offset_y:offset_y + count_y, offset_x:offset_x + count_x].astype(jnp.float32)
                tap_term = jnp.einsum('rwc,co->rwo', window, weight[kernel_y, kernel_x].astype(jnp.float32))
                running = tap_term if running is None else running + tap_term
        return running
    upper_rows = jnp.stack([parity(0, 0), parity(0, 1)], axis=2)
    lower_rows = jnp.stack([parity(1, 0), parity(1, 1)], axis=2)
    merged = jnp.stack([upper_rows, lower_rows], axis=1)
    return merged.reshape(2 * count_y, 2 * count_x, merged.shape[-1])

def feat_pad(values):
    return jnp.pad(values, ((1, 1), (1, 1), (0, 0)))

def network_pass(padded_fields, weights):
    in_weight, down_weight, low_weight, up_weight, fine_weight, out_weight = weights
    top_level = silu_round(conv_fields(padded_fields, in_weight))
    coarse = silu_round(conv_feat(feat_pad(top_level), down_weight, 2))
    middle = silu_round(conv_feat(feat_pad(coarse), low_weight, 1))
    upward = up_conv(feat_pad(middle), up_weight)
    summed = (top_level.astype(jnp.float32) + upward).astype(jnp.bfloat16)
    refined = silu_round(conv_feat(feat_pad(summed), fine_weight, 1))
    return conv_out(feat_pad(refined), out_weight)

def reference(conditioning, member_noise, reg_in, reg_down, reg_low, reg_up, reg_fine, reg_out, dif_in, dif_down, dif_low, dif_up, dif_fine, dif_out):
    field_pad = ((0, 0), (1, 1), (1, 1))
    reg_mean = network_pass(jnp.pad(conditioning, field_pad), (reg_in, reg_down, reg_low, reg_up, reg_fine, reg_out))
    dif_weights = (dif_in, dif_down, dif_low, dif_up, dif_fine, dif_out)

    def member_run(noise_one):
        residual_field = sigma_top * noise_one.astype(jnp.float32)
        for step_index in range(STEPS):
            sigma_now = sigma_top * sigma_ratio ** step_index
            sigma_next = sigma_top * sigma_ratio ** (step_index + 1) if step_index + 1 < STEPS else 0.0
            scale_sq = sigma_now ** 2 + sigma_data ** 2
            in_gain = 1.0 / math_sqrt(scale_sq)
            skip_gain = sigma_data ** 2 / scale_sq
            out_gain = sigma_now * sigma_data / math_sqrt(scale_sq)
            inputs = jnp.concatenate([(in_gain * residual_field).astype(jnp.bfloat16), conditioning, reg_mean.astype(jnp.bfloat16)], axis=0)
            network = network_pass(jnp.pad(inputs, field_pad), dif_weights)
            denoised = skip_gain * residual_field + out_gain * network
            residual_field = residual_field + (sigma_next - sigma_now) / sigma_now * (residual_field - denoised)
        return reg_mean + residual_field
    return lax.map(member_run, member_noise)

def math_sqrt(number):
    return number ** 0.5
```

```python
import jax
import jax.numpy as jnp
from jax import lax
from jax.sharding import PartitionSpec as P

STEPS = 2


sigma_top = 1.0
sigma_ratio = 0.4
sigma_data = 0.5


def from_tile(values, distance):
    count = lax.axis_size("tile")
    pairs = [(i + distance, i) for i in range(count) if 0 <= i + distance < count]
    return lax.ppermute(values, "tile", pairs)


def halo_rows(values, dim, below, above):
    rows = values.shape[dim]
    pieces = []
    need = below
    distance = 1
    while need > 0:
        take = min(need, rows)
        part = lax.slice_in_dim(values, rows - take, rows, axis=dim)
        pieces.insert(0, from_tile(part, -distance))
        need -= take
        distance += 1
    pieces.append(values)
    need = above
    distance = 1
    while need > 0:
        take = min(need, rows)
        part = lax.slice_in_dim(values, 0, take, axis=dim)
        pieces.append(from_tile(part, distance))
        need -= take
        distance += 1
    return jnp.concatenate(pieces, axis=dim)


def row_mask(values, first, base, limit, axis=0):
    shape = [1] * values.ndim
    shape[axis] = values.shape[axis]
    index = base + first + lax.broadcasted_iota(jnp.int32, tuple(shape), axis)
    keep = (index >= 0) & (index < limit)
    return jnp.where(keep, values, jnp.zeros_like(values))


def conv(lhs, rhs, specs, strides=(1, 1), padding=((0, 0), (1, 1)), dilation=(1, 1)):
    return lax.conv_general_dilated(
        lhs,
        rhs,
        window_strides=strides,
        padding=padding,
        lhs_dilation=dilation,
        dimension_numbers=specs,
        preferred_element_type=jnp.float32,
    )


def silu(values):
    return jax.nn.silu(values)


def unet(fields, first, out_lo, out_hi, weights, base, grid_rows):
    w_in, w_down, w_low, w_up, w_fine, w_out = weights
    join_lo, join_hi = out_lo - 2, out_hi + 2
    mid_lo, mid_hi = join_lo // 2 - 1, join_hi // 2 + 1
    crs_lo, crs_hi = mid_lo - 1, mid_hi + 1
    top_lo, top_hi = min(2 * crs_lo - 1, join_lo), max(2 * crs_hi, join_hi)
    in_lo, in_hi = top_lo - 1, top_hi + 1
    assert in_lo >= first and in_hi <= first + fields.shape[1]
    window = fields[:, in_lo - first : in_hi - first][None]
    top = conv(window, w_in, ("NCHW", "HWIO", "NHWC"))[0]
    top = row_mask(silu(top), top_lo, base, grid_rows).astype(jnp.bfloat16)
    down_in = top[2 * crs_lo - 1 - top_lo : 2 * crs_hi - top_lo][None]
    coarse = conv(down_in, w_down, ("NHWC", "HWIO", "NHWC"), strides=(2, 2))[0]
    coarse = row_mask(silu(coarse), crs_lo, base // 2, grid_rows // 2).astype(jnp.bfloat16)
    middle = conv(coarse[None], w_low, ("NHWC", "HWIO", "NHWC"))[0]
    middle = row_mask(silu(middle), mid_lo, base // 2, grid_rows // 2).astype(jnp.bfloat16)
    upward = conv(
        middle[None],
        w_up[::-1, ::-1],
        ("NHWC", "HWIO", "NHWC"),
        padding=((0, 0), (2, 2)),
        dilation=(2, 2),
    )[0]
    joined = top[join_lo - top_lo : join_hi - top_lo].astype(jnp.float32) + upward
    joined = row_mask(joined, join_lo, base, grid_rows).astype(jnp.bfloat16)
    refined = conv(joined[None], w_fine, ("NHWC", "HWIO", "NHWC"))[0]
    refined = row_mask(silu(refined), join_lo + 1, base, grid_rows).astype(jnp.bfloat16)
    return conv(refined[None], w_out, ("NHWC", "HWOI", "NCHW"))[0]


def shards(
    conditioning,
    member_noise,
    reg_in,
    reg_down,
    reg_low,
    reg_up,
    reg_fine,
    reg_out,
    dif_in,
    dif_down,
    dif_low,
    dif_up,
    dif_fine,
    dif_out,
):
    rows = conditioning.shape[1]
    grid_rows = rows * lax.axis_size("tile")
    base = lax.axis_index("tile") * rows
    reg_weights = (reg_in, reg_down, reg_low, reg_up, reg_fine, reg_out)
    dif_weights = (dif_in, dif_down, dif_low, dif_up, dif_fine, dif_out)
    cond_count = conditioning.shape[0]
    noise_count = member_noise.shape[1]

    residual_field = sigma_top * member_noise[0]
    gains = []
    for step_index in range(STEPS):
        sigma_now = sigma_top * sigma_ratio**step_index
        sigma_next = sigma_top * sigma_ratio ** (step_index + 1) if step_index + 1 < STEPS else 0.0
        scale_sq = sigma_now**2 + sigma_data**2
        gains.append(
            (
                1.0 / scale_sq**0.5,
                sigma_data**2 / scale_sq,
                sigma_now * sigma_data / scale_sq**0.5,
                (sigma_next - sigma_now) / sigma_now,
            )
        )

    dif_halo = 8
    reg_halo = 2 * dif_halo
    noise_in = (gains[0][0] * residual_field).astype(jnp.bfloat16)
    near = jnp.concatenate([noise_in, conditioning], axis=0)
    near_wide = halo_rows(near, 1, dif_halo, dif_halo)
    cond_wide = halo_rows(conditioning, 1, reg_halo, reg_halo)

    mean_wide = unet(cond_wide, -reg_halo, -dif_halo, rows + dif_halo, reg_weights, base, grid_rows)
    mean_wide = row_mask(mean_wide, -dif_halo, base, grid_rows, axis=1)
    mean_input = mean_wide.astype(jnp.bfloat16)
    cond_near = near_wide[noise_count:]
    reg_mean = mean_wide[:, dif_halo : dif_halo + rows]

    field_in = near_wide[:noise_count]
    for step_index in range(STEPS):
        in_gain, skip_gain, out_gain, step_gain = gains[step_index]
        if step_index > 0:
            field_in = halo_rows(
                (in_gain * residual_field).astype(jnp.bfloat16), 1, dif_halo, dif_halo
            )
        inputs = jnp.concatenate([field_in, cond_near, mean_input], axis=0)
        network = unet(inputs, -dif_halo, 0, rows, dif_weights, base, grid_rows)
        denoised = skip_gain * residual_field + out_gain * network
        residual_field = residual_field + step_gain * (residual_field - denoised)
    return (reg_mean + residual_field)[None]


def solution(mesh):
    return jax.shard_map(
        shards,
        mesh=mesh,
        in_specs=(
            P(None, "tile", None),
            P("ens", None, "tile", None),
            P(),
            P(),
            P(),
            P(),
            P(),
            P(),
            P(),
            P(),
            P(),
            P(),
            P(),
            P(),
        ),
        out_specs=P("ens", None, "tile", None),
        check_vma=False,
    )
```

```python
import jax
import jax.numpy as jnp
from jax import lax
from jax.sharding import PartitionSpec as P

STEPS = 2


sigma_top = 1.0
sigma_ratio = 0.4
sigma_data = 0.5


def from_tile(values, distance):
    count = lax.axis_size("tile")
    pairs = [(i + distance, i) for i in range(count) if 0 <= i + distance < count]
    return lax.ppermute(values, "tile", pairs)


def halo_rows(values, dim, below, above):
    rows = values.shape[dim]
    pieces = []
    need = below
    distance = 1
    while need > 0:
        take = min(need, rows)
        part = lax.slice_in_dim(values, rows - take, rows, axis=dim)
        pieces.insert(0, from_tile(part, -distance))
        need -= take
        distance += 1
    pieces.append(values)
    need = above
    distance = 1
    while need > 0:
        take = min(need, rows)
        part = lax.slice_in_dim(values, 0, take, axis=dim)
        pieces.append(from_tile(part, distance))
        need -= take
        distance += 1
    return jnp.concatenate(pieces, axis=dim)


def row_mask(values, first, base, limit, axis=0):
    shape = [1] * values.ndim
    shape[axis] = values.shape[axis]
    index = base + first + lax.broadcasted_iota(jnp.int32, tuple(shape), axis)
    keep = (index >= 0) & (index < limit)
    return jnp.where(keep, values, jnp.zeros_like(values))


def conv(lhs, rhs, specs, strides=(1, 1), padding=((0, 0), (1, 1)), dilation=(1, 1)):
    return lax.conv_general_dilated(
        lhs,
        rhs,
        window_strides=strides,
        padding=padding,
        lhs_dilation=dilation,
        dimension_numbers=specs,
        preferred_element_type=jnp.float32,
    )


def silu(values):
    return jax.nn.silu(values)


def unet(fields, first, out_lo, out_hi, weights, base, grid_rows):
    w_in, w_down, w_low, w_up, w_fine, w_out = weights
    join_lo, join_hi = out_lo - 2, out_hi + 2
    mid_lo, mid_hi = join_lo // 2 - 1, join_hi // 2 + 1
    crs_lo, crs_hi = mid_lo - 1, mid_hi + 1
    top_lo, top_hi = min(2 * crs_lo - 1, join_lo), max(2 * crs_hi, join_hi)
    in_lo, in_hi = top_lo - 1, top_hi + 1
    assert in_lo >= first and in_hi <= first + fields.shape[1]
    window = jnp.transpose(fields[:, in_lo - first : in_hi - first], (1, 2, 0))[None]
    top = conv(window, w_in, ("NHWC", "HWIO", "NHWC"))[0]
    top = row_mask(silu(top), top_lo, base, grid_rows).astype(jnp.bfloat16)
    down_in = top[2 * crs_lo - 1 - top_lo : 2 * crs_hi - top_lo][None]
    coarse = conv(down_in, w_down, ("NHWC", "HWIO", "NHWC"), strides=(2, 2))[0]
    coarse = row_mask(silu(coarse), crs_lo, base // 2, grid_rows // 2).astype(jnp.bfloat16)
    middle = conv(coarse[None], w_low, ("NHWC", "HWIO", "NHWC"))[0]
    middle = row_mask(silu(middle), mid_lo, base // 2, grid_rows // 2).astype(jnp.bfloat16)
    upward = conv(
        middle[None],
        w_up[::-1, ::-1],
        ("NHWC", "HWIO", "NHWC"),
        padding=((0, 0), (2, 2)),
        dilation=(2, 2),
    )[0]
    joined = top[join_lo - top_lo : join_hi - top_lo].astype(jnp.float32) + upward
    joined = row_mask(joined, join_lo, base, grid_rows).astype(jnp.bfloat16)
    refined = conv(joined[None], w_fine, ("NHWC", "HWIO", "NHWC"))[0]
    refined = row_mask(silu(refined), join_lo + 1, base, grid_rows).astype(jnp.bfloat16)
    out_count = w_out.shape[2]
    lanes = w_out.shape[3]
    w_wide = jnp.pad(w_out, ((0, 0), (0, 0), (0, lanes - out_count), (0, 0)))
    result = conv(refined[None], w_wide, ("NHWC", "HWOI", "NHWC"))[0]
    return jnp.transpose(result[..., :out_count], (2, 0, 1))


def shards(
    conditioning,
    member_noise,
    reg_in,
    reg_down,
    reg_low,
    reg_up,
    reg_fine,
    reg_out,
    dif_in,
    dif_down,
    dif_low,
    dif_up,
    dif_fine,
    dif_out,
):
    rows = conditioning.shape[1]
    grid_rows = rows * lax.axis_size("tile")
    base = lax.axis_index("tile") * rows
    reg_weights = (reg_in, reg_down, reg_low, reg_up, reg_fine, reg_out)
    dif_weights = (dif_in, dif_down, dif_low, dif_up, dif_fine, dif_out)
    cond_count = conditioning.shape[0]
    noise_count = member_noise.shape[1]

    residual_field = sigma_top * member_noise[0]
    gains = []
    for step_index in range(STEPS):
        sigma_now = sigma_top * sigma_ratio**step_index
        sigma_next = sigma_top * sigma_ratio ** (step_index + 1) if step_index + 1 < STEPS else 0.0
        scale_sq = sigma_now**2 + sigma_data**2
        gains.append(
            (
                1.0 / scale_sq**0.5,
                sigma_data**2 / scale_sq,
                sigma_now * sigma_data / scale_sq**0.5,
                (sigma_next - sigma_now) / sigma_now,
            )
        )

    dif_halo = 8
    reg_halo = 2 * dif_halo
    noise_in = (gains[0][0] * residual_field).astype(jnp.bfloat16)
    near = jnp.concatenate([noise_in, conditioning], axis=0)
    if rows == dif_halo:
        near_below = from_tile(near, -1)
        near_above = from_tile(near, 1)
        near_wide = jnp.concatenate([near_below, near, near_above], axis=1)
        cond_wide = jnp.concatenate(
            [
                from_tile(conditioning, -2),
                near_wide[noise_count:],
                from_tile(conditioning, 2),
            ],
            axis=1,
        )
    else:
        near_wide = halo_rows(near, 1, dif_halo, dif_halo)
        cond_wide = halo_rows(conditioning, 1, reg_halo, reg_halo)

    mean_wide = unet(cond_wide, -reg_halo, -dif_halo, rows + dif_halo, reg_weights, base, grid_rows)
    mean_wide = row_mask(mean_wide, -dif_halo, base, grid_rows, axis=1)
    mean_input = mean_wide.astype(jnp.bfloat16)
    cond_near = near_wide[noise_count:]
    reg_mean = mean_wide[:, dif_halo : dif_halo + rows]

    field_in = near_wide[:noise_count]
    for step_index in range(STEPS):
        in_gain, skip_gain, out_gain, step_gain = gains[step_index]
        if step_index > 0:
            field_in = halo_rows(
                (in_gain * residual_field).astype(jnp.bfloat16), 1, dif_halo, dif_halo
            )
        inputs = jnp.concatenate([field_in, cond_near, mean_input], axis=0)
        network = unet(inputs, -dif_halo, 0, rows, dif_weights, base, grid_rows)
        denoised = skip_gain * residual_field + out_gain * network
        residual_field = residual_field + step_gain * (residual_field - denoised)
    return (reg_mean + residual_field)[None]


def solution(mesh):
    return jax.shard_map(
        shards,
        mesh=mesh,
        in_specs=(
            P(None, "tile", None),
            P("ens", None, "tile", None),
            P(),
            P(),
            P(),
            P(),
            P(),
            P(),
            P(),
            P(),
            P(),
            P(),
            P(),
            P(),
        ),
        out_specs=P("ens", None, "tile", None),
        check_vma=False,
    )
```

```python
import jax
import jax.numpy as jnp
from jax import lax
from jax.sharding import PartitionSpec as P

STEPS = 2


sigma_top = 1.0
sigma_ratio = 0.4
sigma_data = 0.5


def from_tile(values, distance):
    count = lax.axis_size("tile")
    pairs = [(i + distance, i) for i in range(count) if 0 <= i + distance < count]
    return lax.ppermute(values, "tile", pairs)


def halo_rows(values, dim, below, above):
    rows = values.shape[dim]
    pieces = []
    need = below
    distance = 1
    while need > 0:
        take = min(need, rows)
        part = lax.slice_in_dim(values, rows - take, rows, axis=dim)
        pieces.insert(0, from_tile(part, -distance))
        need -= take
        distance += 1
    pieces.append(values)
    need = above
    distance = 1
    while need > 0:
        take = min(need, rows)
        part = lax.slice_in_dim(values, 0, take, axis=dim)
        pieces.append(from_tile(part, distance))
        need -= take
        distance += 1
    return jnp.concatenate(pieces, axis=dim)


def row_mask(values, first, base, limit, axis=0):
    shape = [1] * values.ndim
    shape[axis] = values.shape[axis]
    index = base + first + lax.broadcasted_iota(jnp.int32, tuple(shape), axis)
    keep = (index >= 0) & (index < limit)
    return jnp.where(keep, values, jnp.zeros_like(values))


def conv(lhs, rhs, specs, strides=(1, 1), padding=((0, 0), (1, 1)), dilation=(1, 1)):
    return lax.conv_general_dilated(
        lhs,
        rhs,
        window_strides=strides,
        padding=padding,
        lhs_dilation=dilation,
        dimension_numbers=specs,
        preferred_element_type=jnp.float32,
    )


def silu(values):
    return jax.nn.silu(values)


def windows(out_lo, out_hi):
    join_lo, join_hi = out_lo - 2, out_hi + 2
    mid_lo, mid_hi = join_lo // 2 - 1, join_hi // 2 + 1
    crs_lo, crs_hi = mid_lo - 1, mid_hi + 1
    top_lo, top_hi = min(2 * crs_lo - 1, join_lo), max(2 * crs_hi, join_hi)
    return join_lo, join_hi, mid_lo, mid_hi, crs_lo, crs_hi, top_lo, top_hi


def conv_in(fields, first, out_lo, out_hi, weight):
    count, _, cols = fields.shape
    lo, hi = out_lo - 1 - first, out_hi + 1 - first
    assert lo >= 0 and hi <= fields.shape[1]
    padded = jnp.pad(fields[:, lo:hi], ((0, 0), (0, 0), (1, 1)))
    rows = out_hi - out_lo
    patches = jnp.concatenate(
        [padded[:, ty : ty + rows, tx : tx + cols] for ty in range(3) for tx in range(3)], axis=0
    )
    flat = weight.reshape(9 * count, weight.shape[3])
    return jnp.einsum("krw,ko->rwo", patches, flat, preferred_element_type=jnp.float32)


def unet(fields, first, out_lo, out_hi, weights, base, grid_rows, top_extra=None):
    w_in, w_down, w_low, w_up, w_fine, w_out = weights
    join_lo, join_hi, mid_lo, mid_hi, crs_lo, crs_hi, top_lo, top_hi = windows(out_lo, out_hi)
    top = conv_in(fields, first, top_lo, top_hi, w_in[:, :, : fields.shape[0]])
    if top_extra is not None:
        top = top + top_extra
    top = row_mask(silu(top), top_lo, base, grid_rows).astype(jnp.bfloat16)
    down_in = top[2 * crs_lo - 1 - top_lo : 2 * crs_hi - top_lo][None]
    coarse = conv(down_in, w_down, ("NHWC", "HWIO", "NHWC"), strides=(2, 2))[0]
    coarse = row_mask(silu(coarse), crs_lo, base // 2, grid_rows // 2).astype(jnp.bfloat16)
    middle = conv(coarse[None], w_low, ("NHWC", "HWIO", "NHWC"))[0]
    middle = row_mask(silu(middle), mid_lo, base // 2, grid_rows // 2).astype(jnp.bfloat16)
    upward = conv(
        middle[None],
        w_up[::-1, ::-1],
        ("NHWC", "HWIO", "NHWC"),
        padding=((0, 0), (2, 2)),
        dilation=(2, 2),
    )[0]
    joined = top[join_lo - top_lo : join_hi - top_lo].astype(jnp.float32) + upward
    joined = row_mask(joined, join_lo, base, grid_rows).astype(jnp.bfloat16)
    refined = conv(joined[None], w_fine, ("NHWC", "HWIO", "NHWC"))[0]
    refined = row_mask(silu(refined), join_lo + 1, base, grid_rows).astype(jnp.bfloat16)
    out_count = w_out.shape[2]
    lanes = w_out.shape[3]
    w_wide = jnp.pad(w_out, ((0, 0), (0, 0), (0, lanes - out_count), (0, 0)))
    result = conv(refined[None], w_wide, ("NHWC", "HWOI", "NHWC"))[0]
    return jnp.transpose(result[..., :out_count], (2, 0, 1))


def shards(
    conditioning,
    member_noise,
    reg_in,
    reg_down,
    reg_low,
    reg_up,
    reg_fine,
    reg_out,
    dif_in,
    dif_down,
    dif_low,
    dif_up,
    dif_fine,
    dif_out,
):
    rows = conditioning.shape[1]
    grid_rows = rows * lax.axis_size("tile")
    base = lax.axis_index("tile") * rows
    reg_weights = (reg_in, reg_down, reg_low, reg_up, reg_fine, reg_out)
    dif_weights = (dif_in, dif_down, dif_low, dif_up, dif_fine, dif_out)
    cond_count = conditioning.shape[0]
    noise_count = member_noise.shape[1]

    residual_field = sigma_top * member_noise[0]
    gains = []
    for step_index in range(STEPS):
        sigma_now = sigma_top * sigma_ratio**step_index
        sigma_next = sigma_top * sigma_ratio ** (step_index + 1) if step_index + 1 < STEPS else 0.0
        scale_sq = sigma_now**2 + sigma_data**2
        gains.append(
            (
                1.0 / scale_sq**0.5,
                sigma_data**2 / scale_sq,
                sigma_now * sigma_data / scale_sq**0.5,
                (sigma_next - sigma_now) / sigma_now,
            )
        )

    dif_halo = 8
    reg_halo = 2 * dif_halo
    noise_in = (gains[0][0] * residual_field).astype(jnp.bfloat16)
    near = jnp.concatenate([noise_in, conditioning], axis=0)
    if rows == dif_halo:
        near_below = from_tile(near, -1)
        near_above = from_tile(near, 1)
        near_wide = jnp.concatenate([near_below, near, near_above], axis=1)
        cond_wide = jnp.concatenate(
            [
                from_tile(conditioning, -2),
                near_wide[noise_count:],
                from_tile(conditioning, 2),
            ],
            axis=1,
        )
    else:
        near_wide = halo_rows(near, 1, dif_halo, dif_halo)
        cond_wide = halo_rows(conditioning, 1, reg_halo, reg_halo)

    mean_wide = unet(cond_wide, -reg_halo, -dif_halo, rows + dif_halo, reg_weights, base, grid_rows)
    mean_wide = row_mask(mean_wide, -dif_halo, base, grid_rows, axis=1)
    mean_input = mean_wide.astype(jnp.bfloat16)
    cond_near = near_wide[noise_count:]
    reg_mean = mean_wide[:, dif_halo : dif_halo + rows]

    dif_top_lo, dif_top_hi = windows(0, rows)[6:]
    fixed_in = jnp.concatenate([cond_near, mean_input], axis=0)
    fixed_top = conv_in(
        fixed_in, -dif_halo, dif_top_lo, dif_top_hi, dif_in[:, :, noise_count:]
    )
    field_in = near_wide[:noise_count]
    for step_index in range(STEPS):
        in_gain, skip_gain, out_gain, step_gain = gains[step_index]
        if step_index > 0:
            field_in = halo_rows(
                (in_gain * residual_field).astype(jnp.bfloat16), 1, dif_halo, dif_halo
            )
        network = unet(
            field_in, -dif_halo, 0, rows, dif_weights, base, grid_rows, top_extra=fixed_top
        )
        denoised = skip_gain * residual_field + out_gain * network
        residual_field = residual_field + step_gain * (residual_field - denoised)
    return (reg_mean + residual_field)[None]


def solution(mesh):
    return jax.shard_map(
        shards,
        mesh=mesh,
        in_specs=(
            P(None, "tile", None),
            P("ens", None, "tile", None),
            P(),
            P(),
            P(),
            P(),
            P(),
            P(),
            P(),
            P(),
            P(),
            P(),
            P(),
            P(),
        ),
        out_specs=P("ens", None, "tile", None),
        check_vma=False,
    )
```

```python
import jax
import jax.numpy as jnp
from jax import lax
from jax.sharding import PartitionSpec as P

STEPS = 2


sigma_top = 1.0
sigma_ratio = 0.4
sigma_data = 0.5


def from_tile(values, distance):
    count = lax.axis_size("tile")
    pairs = [(i + distance, i) for i in range(count) if 0 <= i + distance < count]
    return lax.ppermute(values, "tile", pairs)


def halo_rows(values, dim, below, above):
    rows = values.shape[dim]
    pieces = []
    need = below
    distance = 1
    while need > 0:
        take = min(need, rows)
        part = lax.slice_in_dim(values, rows - take, rows, axis=dim)
        pieces.insert(0, from_tile(part, -distance))
        need -= take
        distance += 1
    pieces.append(values)
    need = above
    distance = 1
    while need > 0:
        take = min(need, rows)
        part = lax.slice_in_dim(values, 0, take, axis=dim)
        pieces.append(from_tile(part, distance))
        need -= take
        distance += 1
    return jnp.concatenate(pieces, axis=dim)


def row_mask(values, first, base, limit, axis=0):
    shape = [1] * values.ndim
    shape[axis] = values.shape[axis]
    index = base + first + lax.broadcasted_iota(jnp.int32, tuple(shape), axis)
    keep = (index >= 0) & (index < limit)
    return jnp.where(keep, values, jnp.zeros_like(values))


def conv(lhs, rhs, specs, strides=(1, 1), padding=((0, 0), (1, 1)), dilation=(1, 1)):
    return lax.conv_general_dilated(
        lhs,
        rhs,
        window_strides=strides,
        padding=padding,
        lhs_dilation=dilation,
        dimension_numbers=specs,
        preferred_element_type=jnp.float32,
    )


def silu(values):
    return jax.nn.silu(values)


def windows(out_lo, out_hi):
    join_lo, join_hi = out_lo - 2, out_hi + 2
    mid_lo, mid_hi = join_lo // 2 - 1, join_hi // 2 + 1
    crs_lo, crs_hi = mid_lo - 1, mid_hi + 1
    top_lo, top_hi = min(2 * crs_lo - 1, join_lo), max(2 * crs_hi, join_hi)
    return join_lo, join_hi, mid_lo, mid_hi, crs_lo, crs_hi, top_lo, top_hi


def conv_in(fields, first, out_lo, out_hi, weight):
    count, _, cols = fields.shape
    lo, hi = out_lo - 1 - first, out_hi + 1 - first
    assert lo >= 0 and hi <= fields.shape[1]
    extra = -count % 16
    weight = jnp.pad(weight, ((0, 0), (0, 0), (0, extra), (0, 0)))
    padded = jnp.pad(fields[:, lo:hi], ((0, extra), (0, 0), (1, 1)))
    count += extra
    rows = out_hi - out_lo
    patches = jnp.concatenate(
        [padded[:, ty : ty + rows, tx : tx + cols] for ty in range(3) for tx in range(3)], axis=0
    )
    flat = weight.reshape(9 * count, weight.shape[3])
    return jnp.einsum("krw,ko->rwo", patches, flat, preferred_element_type=jnp.float32)


def unet(fields, first, out_lo, out_hi, weights, base, grid_rows, top_extra=None):
    w_in, w_down, w_low, w_up, w_fine, w_out = weights
    join_lo, join_hi, mid_lo, mid_hi, crs_lo, crs_hi, top_lo, top_hi = windows(out_lo, out_hi)
    top = conv_in(fields, first, top_lo, top_hi, w_in[:, :, : fields.shape[0]])
    if top_extra is not None:
        top = top + top_extra
    top = row_mask(silu(top), top_lo, base, grid_rows).astype(jnp.bfloat16)
    down_in = top[2 * crs_lo - 1 - top_lo : 2 * crs_hi - top_lo][None]
    coarse = conv(down_in, w_down, ("NHWC", "HWIO", "NHWC"), strides=(2, 2))[0]
    coarse = row_mask(silu(coarse), crs_lo, base // 2, grid_rows // 2).astype(jnp.bfloat16)
    middle = conv(coarse[None], w_low, ("NHWC", "HWIO", "NHWC"))[0]
    middle = row_mask(silu(middle), mid_lo, base // 2, grid_rows // 2).astype(jnp.bfloat16)
    upward = conv(
        middle[None],
        w_up[::-1, ::-1],
        ("NHWC", "HWIO", "NHWC"),
        padding=((0, 0), (2, 2)),
        dilation=(2, 2),
    )[0]
    joined = top[join_lo - top_lo : join_hi - top_lo].astype(jnp.float32) + upward
    joined = row_mask(joined, join_lo, base, grid_rows).astype(jnp.bfloat16)
    refined = conv(joined[None], w_fine, ("NHWC", "HWIO", "NHWC"))[0]
    refined = row_mask(silu(refined), join_lo + 1, base, grid_rows).astype(jnp.bfloat16)
    return conv_out(refined, w_out)


def conv_out(refined, weight):
    count, cols = refined.shape[0] - 2, refined.shape[1]
    outs = weight.shape[2]
    flat = weight.reshape(9 * outs, weight.shape[3])
    planes = jnp.einsum("tc,rwc->trw", flat, refined, preferred_element_type=jnp.float32)
    planes = jnp.pad(planes, ((0, 0), (0, 0), (1, 1)))
    total = None
    for ty in range(3):
        for tx in range(3):
            tap = (ty * 3 + tx) * outs
            term = planes[tap : tap + outs, ty : ty + count, tx : tx + cols]
            total = term if total is None else total + term
    return total


def shards(
    conditioning,
    member_noise,
    reg_in,
    reg_down,
    reg_low,
    reg_up,
    reg_fine,
    reg_out,
    dif_in,
    dif_down,
    dif_low,
    dif_up,
    dif_fine,
    dif_out,
):
    rows = conditioning.shape[1]
    grid_rows = rows * lax.axis_size("tile")
    base = lax.axis_index("tile") * rows
    reg_weights = (reg_in, reg_down, reg_low, reg_up, reg_fine, reg_out)
    dif_weights = (dif_in, dif_down, dif_low, dif_up, dif_fine, dif_out)
    cond_count = conditioning.shape[0]
    noise_count = member_noise.shape[1]

    residual_field = sigma_top * member_noise[0]
    gains = []
    for step_index in range(STEPS):
        sigma_now = sigma_top * sigma_ratio**step_index
        sigma_next = sigma_top * sigma_ratio ** (step_index + 1) if step_index + 1 < STEPS else 0.0
        scale_sq = sigma_now**2 + sigma_data**2
        gains.append(
            (
                1.0 / scale_sq**0.5,
                sigma_data**2 / scale_sq,
                sigma_now * sigma_data / scale_sq**0.5,
                (sigma_next - sigma_now) / sigma_now,
            )
        )

    dif_halo = 8
    reg_halo = 2 * dif_halo
    noise_in = (gains[0][0] * residual_field).astype(jnp.bfloat16)
    near = jnp.concatenate([noise_in, conditioning], axis=0)
    if rows == dif_halo:
        near_below = from_tile(near, -1)
        near_above = from_tile(near, 1)
        near_wide = jnp.concatenate([near_below, near, near_above], axis=1)
        cond_wide = jnp.concatenate(
            [
                from_tile(conditioning, -2),
                near_wide[noise_count:],
                from_tile(conditioning, 2),
            ],
            axis=1,
        )
    else:
        near_wide = halo_rows(near, 1, dif_halo, dif_halo)
        cond_wide = halo_rows(conditioning, 1, reg_halo, reg_halo)

    mean_wide = unet(cond_wide, -reg_halo, -dif_halo, rows + dif_halo, reg_weights, base, grid_rows)
    mean_wide = row_mask(mean_wide, -dif_halo, base, grid_rows, axis=1)
    mean_input = mean_wide.astype(jnp.bfloat16)
    cond_near = near_wide[noise_count:]
    reg_mean = mean_wide[:, dif_halo : dif_halo + rows]

    dif_top_lo, dif_top_hi = windows(0, rows)[6:]
    fixed_in = jnp.concatenate([cond_near, mean_input], axis=0)
    fixed_top = conv_in(
        fixed_in, -dif_halo, dif_top_lo, dif_top_hi, dif_in[:, :, noise_count:]
    )
    field_in = near_wide[:noise_count]
    for step_index in range(STEPS):
        in_gain, skip_gain, out_gain, step_gain = gains[step_index]
        if step_index > 0:
            field_in = halo_rows(
                (in_gain * residual_field).astype(jnp.bfloat16), 1, dif_halo, dif_halo
            )
        network = unet(
            field_in, -dif_halo, 0, rows, dif_weights, base, grid_rows, top_extra=fixed_top
        )
        denoised = skip_gain * residual_field + out_gain * network
        residual_field = residual_field + step_gain * (residual_field - denoised)
    return (reg_mean + residual_field)[None]


def solution(mesh):
    return jax.shard_map(
        shards,
        mesh=mesh,
        in_specs=(
            P(None, "tile", None),
            P("ens", None, "tile", None),
            P(),
            P(),
            P(),
            P(),
            P(),
            P(),
            P(),
            P(),
            P(),
            P(),
            P(),
            P(),
        ),
        out_specs=P("ens", None, "tile", None),
        check_vma=False,
    )
```

```python
import jax
import jax.numpy as jnp
from jax import lax
from jax.sharding import PartitionSpec as P

STEPS = 2


sigma_top = 1.0
sigma_ratio = 0.4
sigma_data = 0.5


def from_tile(values, distance):
    count = lax.axis_size("tile")
    pairs = [(i + distance, i) for i in range(count) if 0 <= i + distance < count]
    return lax.ppermute(values, "tile", pairs)


def halo_rows(values, dim, below, above):
    rows = values.shape[dim]
    pieces = []
    need = below
    distance = 1
    while need > 0:
        take = min(need, rows)
        part = lax.slice_in_dim(values, rows - take, rows, axis=dim)
        pieces.insert(0, from_tile(part, -distance))
        need -= take
        distance += 1
    pieces.append(values)
    need = above
    distance = 1
    while need > 0:
        take = min(need, rows)
        part = lax.slice_in_dim(values, 0, take, axis=dim)
        pieces.append(from_tile(part, distance))
        need -= take
        distance += 1
    return jnp.concatenate(pieces, axis=dim)


def row_mask(values, first, base, limit, axis=0):
    shape = [1] * values.ndim
    shape[axis] = values.shape[axis]
    index = base + first + lax.broadcasted_iota(jnp.int32, tuple(shape), axis)
    keep = (index >= 0) & (index < limit)
    return jnp.where(keep, values, jnp.zeros_like(values))


def conv(lhs, rhs, specs, strides=(1, 1), padding=((0, 0), (1, 1)), dilation=(1, 1)):
    return lax.conv_general_dilated(
        lhs,
        rhs,
        window_strides=strides,
        padding=padding,
        lhs_dilation=dilation,
        dimension_numbers=specs,
        preferred_element_type=jnp.float32,
    )


def silu(values):
    return jax.nn.silu(values)


def windows(out_lo, out_hi):
    join_lo, join_hi = out_lo - 2, out_hi + 2
    mid_lo, mid_hi = join_lo // 2 - 1, join_hi // 2 + 1
    crs_lo, crs_hi = mid_lo - 1, mid_hi + 1
    top_lo, top_hi = min(2 * crs_lo - 1, join_lo), max(2 * crs_hi, join_hi)
    return join_lo, join_hi, mid_lo, mid_hi, crs_lo, crs_hi, top_lo, top_hi


def conv_in(fields, first, out_lo, out_hi, weight):
    count, _, cols = fields.shape
    lo, hi = out_lo - 1 - first, out_hi + 1 - first
    assert lo >= 0 and hi <= fields.shape[1]
    extra = -count % 16
    weight = jnp.pad(weight, ((0, 0), (0, 0), (0, extra), (0, 0)))
    padded = jnp.pad(fields[:, lo:hi], ((0, extra), (0, 0), (1, 1)))
    count += extra
    rows = out_hi - out_lo
    patches = jnp.concatenate(
        [padded[:, ty : ty + rows, tx : tx + cols] for ty in range(3) for tx in range(3)], axis=0
    )
    flat = weight.reshape(9 * count, weight.shape[3])
    return jnp.einsum("krw,ko->rwo", patches, flat, preferred_element_type=jnp.float32)


def unet(fields, first, out_lo, out_hi, weights, base, grid_rows, top_extra=None):
    w_in, w_down, w_low, w_up, w_fine, w_out = weights
    join_lo, join_hi, mid_lo, mid_hi, crs_lo, crs_hi, top_lo, top_hi = windows(out_lo, out_hi)
    top = conv_in(fields, first, top_lo, top_hi, w_in[:, :, : fields.shape[0]])
    if top_extra is not None:
        top = top + top_extra
    top = row_mask(silu(top), top_lo, base, grid_rows).astype(jnp.bfloat16)
    down_in = top[2 * crs_lo - 1 - top_lo : 2 * crs_hi - top_lo][None]
    coarse = conv(down_in, w_down, ("NHWC", "HWIO", "NHWC"), strides=(2, 2))[0]
    coarse = row_mask(silu(coarse), crs_lo, base // 2, grid_rows // 2).astype(jnp.bfloat16)
    middle = conv(coarse[None], w_low, ("NHWC", "HWIO", "NHWC"))[0]
    middle = row_mask(silu(middle), mid_lo, base // 2, grid_rows // 2).astype(jnp.bfloat16)
    upward = conv(
        middle[None],
        w_up,
        ("NHWC", "HWIO", "NHWC"),
        padding=((0, 0), (2, 2)),
        dilation=(2, 2),
    )[0]
    joined = top[join_lo - top_lo : join_hi - top_lo].astype(jnp.float32) + upward
    joined = row_mask(joined, join_lo, base, grid_rows).astype(jnp.bfloat16)
    refined = conv(joined[None], w_fine, ("NHWC", "HWIO", "NHWC"))[0]
    refined = row_mask(silu(refined), join_lo + 1, base, grid_rows).astype(jnp.bfloat16)
    return conv_out(refined, w_out)


def conv_out(refined, flat):
    count, cols = refined.shape[0] - 2, refined.shape[1]
    outs = flat.shape[0] // 9
    planes = jnp.einsum("tc,rwc->trw", flat, refined, preferred_element_type=jnp.float32)
    planes = jnp.pad(planes, ((0, 0), (0, 0), (1, 1)))
    total = None
    for ty in range(3):
        for tx in range(3):
            tap = (ty * 3 + tx) * outs
            term = planes[tap : tap + outs, ty : ty + count, tx : tx + cols]
            total = term if total is None else total + term
    return total


def shards(
    conditioning,
    member_noise,
    reg_in,
    reg_down,
    reg_low,
    reg_up,
    reg_fine,
    reg_out,
    dif_in,
    dif_down,
    dif_low,
    dif_up,
    dif_fine,
    dif_out,
):
    rows = conditioning.shape[1]
    grid_rows = rows * lax.axis_size("tile")
    base = lax.axis_index("tile") * rows
    keep = base >= 0

    def staged(weights):
        w_in, w_down, w_low, w_up, w_fine, w_out = weights
        inner = (
            w_down,
            w_low,
            w_up[::-1, ::-1],
            w_fine,
            w_out.reshape(9 * w_out.shape[2], w_out.shape[3]),
        )
        inner = tuple(jnp.where(keep, w, jnp.zeros_like(w)) for w in inner)
        return (w_in,) + lax.optimization_barrier(inner)

    reg_weights = staged((reg_in, reg_down, reg_low, reg_up, reg_fine, reg_out))
    dif_weights = staged((dif_in, dif_down, dif_low, dif_up, dif_fine, dif_out))
    cond_count = conditioning.shape[0]
    noise_count = member_noise.shape[1]

    residual_field = sigma_top * member_noise[0]
    gains = []
    for step_index in range(STEPS):
        sigma_now = sigma_top * sigma_ratio**step_index
        sigma_next = sigma_top * sigma_ratio ** (step_index + 1) if step_index + 1 < STEPS else 0.0
        scale_sq = sigma_now**2 + sigma_data**2
        gains.append(
            (
                1.0 / scale_sq**0.5,
                sigma_data**2 / scale_sq,
                sigma_now * sigma_data / scale_sq**0.5,
                (sigma_next - sigma_now) / sigma_now,
            )
        )

    dif_halo = 8
    reg_halo = 2 * dif_halo
    noise_in = (gains[0][0] * residual_field).astype(jnp.bfloat16)
    near = jnp.concatenate([noise_in, conditioning], axis=0)
    if rows == dif_halo:
        near_below = from_tile(near, -1)
        near_above = from_tile(near, 1)
        near_wide = jnp.concatenate([near_below, near, near_above], axis=1)
        cond_wide = jnp.concatenate(
            [
                from_tile(conditioning, -2),
                near_wide[noise_count:],
                from_tile(conditioning, 2),
            ],
            axis=1,
        )
    else:
        near_wide = halo_rows(near, 1, dif_halo, dif_halo)
        cond_wide = halo_rows(conditioning, 1, reg_halo, reg_halo)

    mean_wide = unet(cond_wide, -reg_halo, -dif_halo, rows + dif_halo, reg_weights, base, grid_rows)
    mean_wide = row_mask(mean_wide, -dif_halo, base, grid_rows, axis=1)
    mean_input = mean_wide.astype(jnp.bfloat16)
    cond_near = near_wide[noise_count:]
    reg_mean = mean_wide[:, dif_halo : dif_halo + rows]

    dif_top_lo, dif_top_hi = windows(0, rows)[6:]
    fixed_in = jnp.concatenate([cond_near, mean_input], axis=0)
    fixed_top = conv_in(
        fixed_in, -dif_halo, dif_top_lo, dif_top_hi, dif_in[:, :, noise_count:]
    )
    field_in = near_wide[:noise_count]
    for step_index in range(STEPS):
        in_gain, skip_gain, out_gain, step_gain = gains[step_index]
        if step_index > 0:
            field_in = halo_rows(
                (in_gain * residual_field).astype(jnp.bfloat16), 1, dif_halo, dif_halo
            )
        network = unet(
            field_in, -dif_halo, 0, rows, dif_weights, base, grid_rows, top_extra=fixed_top
        )
        denoised = skip_gain * residual_field + out_gain * network
        residual_field = residual_field + step_gain * (residual_field - denoised)
    return (reg_mean + residual_field)[None]


def solution(mesh):
    return jax.shard_map(
        shards,
        mesh=mesh,
        in_specs=(
            P(None, "tile", None),
            P("ens", None, "tile", None),
            P(),
            P(),
            P(),
            P(),
            P(),
            P(),
            P(),
            P(),
            P(),
            P(),
            P(),
            P(),
        ),
        out_specs=P("ens", None, "tile", None),
        check_vma=False,
    )
```

```python
import jax
import jax.numpy as jnp
from jax import lax
from jax.sharding import PartitionSpec as P

STEPS = 2


sigma_top = 1.0
sigma_ratio = 0.4
sigma_data = 0.5


def from_tile(values, distance):
    count = lax.axis_size("tile")
    pairs = [(i + distance, i) for i in range(count) if 0 <= i + distance < count]
    return lax.ppermute(values, "tile", pairs)


def halo_rows(values, dim, below, above):
    rows = values.shape[dim]
    pieces = []
    need = below
    distance = 1
    while need > 0:
        take = min(need, rows)
        part = lax.slice_in_dim(values, rows - take, rows, axis=dim)
        pieces.insert(0, from_tile(part, -distance))
        need -= take
        distance += 1
    pieces.append(values)
    need = above
    distance = 1
    while need > 0:
        take = min(need, rows)
        part = lax.slice_in_dim(values, 0, take, axis=dim)
        pieces.append(from_tile(part, distance))
        need -= take
        distance += 1
    return jnp.concatenate(pieces, axis=dim)


def row_mask(values, first, base, limit, axis=0):
    shape = [1] * values.ndim
    shape[axis] = values.shape[axis]
    index = base + first + lax.broadcasted_iota(jnp.int32, tuple(shape), axis)
    keep = (index >= 0) & (index < limit)
    return jnp.where(keep, values, jnp.zeros_like(values))


def conv(lhs, rhs, specs, strides=(1, 1), padding=((0, 0), (1, 1)), dilation=(1, 1)):
    return lax.conv_general_dilated(
        lhs,
        rhs,
        window_strides=strides,
        padding=padding,
        lhs_dilation=dilation,
        dimension_numbers=specs,
        preferred_element_type=jnp.float32,
    )


def silu(values):
    return jax.nn.silu(values)


def windows(out_lo, out_hi):
    join_lo, join_hi = out_lo - 2, out_hi + 2
    mid_lo, mid_hi = join_lo // 2 - 1, join_hi // 2 + 1
    crs_lo, crs_hi = mid_lo - 1, mid_hi + 1
    top_lo, top_hi = min(2 * crs_lo - 1, join_lo), max(2 * crs_hi, join_hi)
    return join_lo, join_hi, mid_lo, mid_hi, crs_lo, crs_hi, top_lo, top_hi


def conv_in(fields, first, out_lo, out_hi, weight):
    count, _, cols = fields.shape
    lo, hi = out_lo - 1 - first, out_hi + 1 - first
    assert lo >= 0 and hi <= fields.shape[1]
    extra = -count % 16
    weight = jnp.pad(weight, ((0, 0), (0, 0), (0, extra), (0, 0)))
    padded = jnp.pad(fields[:, lo:hi], ((0, extra), (0, 0), (1, 1)))
    count += extra
    rows = out_hi - out_lo
    patches = jnp.concatenate(
        [padded[:, ty : ty + rows, tx : tx + cols] for ty in range(3) for tx in range(3)], axis=0
    )
    flat = weight.reshape(9 * count, weight.shape[3])
    return jnp.einsum("krw,ko->rwo", patches, flat, preferred_element_type=jnp.float32)


def unet(fields, first, out_lo, out_hi, weights, base, grid_rows, top_extra=None):
    w_in, w_down, w_low, w_up, w_fine, w_out = weights
    join_lo, join_hi, mid_lo, mid_hi, crs_lo, crs_hi, top_lo, top_hi = windows(out_lo, out_hi)
    top = conv_in(fields, first, top_lo, top_hi, w_in[:, :, : fields.shape[0]])
    if top_extra is not None:
        top = top + top_extra
    top = row_mask(silu(top), top_lo, base, grid_rows).astype(jnp.bfloat16)
    down_in = top[2 * crs_lo - 1 - top_lo : 2 * crs_hi - top_lo][None]
    coarse = conv(down_in, w_down, ("NHWC", "HWIO", "NHWC"), strides=(2, 2))[0]
    coarse = row_mask(silu(coarse), crs_lo, base // 2, grid_rows // 2).astype(jnp.bfloat16)
    middle = conv(coarse[None], w_low, ("NHWC", "HWIO", "NHWC"))[0]
    middle = row_mask(silu(middle), mid_lo, base // 2, grid_rows // 2).astype(jnp.bfloat16)
    upward = conv(
        middle[None],
        w_up,
        ("NHWC", "HWIO", "NHWC"),
        padding=((0, 0), (2, 2)),
        dilation=(2, 2),
    )[0]
    joined = top[join_lo - top_lo : join_hi - top_lo].astype(jnp.float32) + upward
    joined = row_mask(joined, join_lo, base, grid_rows).astype(jnp.bfloat16)
    refined = conv(joined[None], w_fine, ("NHWC", "HWIO", "NHWC"))[0]
    refined = row_mask(silu(refined), join_lo + 1, base, grid_rows).astype(jnp.bfloat16)
    return conv_out(refined, w_out)


def conv_out(refined, flat):
    count, cols = refined.shape[0] - 2, refined.shape[1]
    outs = flat.shape[0] // 9
    planes = jnp.einsum("tc,rwc->trw", flat, refined, preferred_element_type=jnp.float32)
    planes = jnp.pad(planes, ((0, 0), (0, 0), (1, 1)))
    total = None
    for ty in range(3):
        for tx in range(3):
            tap = (ty * 3 + tx) * outs
            term = planes[tap : tap + outs, ty : ty + count, tx : tx + cols]
            total = term if total is None else total + term
    return total


def shards(
    conditioning,
    member_noise,
    reg_in,
    reg_down,
    reg_low,
    reg_up,
    reg_fine,
    reg_out,
    dif_in,
    dif_down,
    dif_low,
    dif_up,
    dif_fine,
    dif_out,
):
    rows = conditioning.shape[1]
    grid_rows = rows * lax.axis_size("tile")
    base = lax.axis_index("tile") * rows
    keep = base >= 0

    def staged(weights):
        w_in, w_down, w_low, w_up, w_fine, w_out = weights
        inner = (
            w_down,
            w_low,
            w_up[::-1, ::-1],
            w_fine,
            w_out.reshape(9 * w_out.shape[2], w_out.shape[3]),
        )
        inner = tuple(jnp.where(keep, w, jnp.zeros_like(w)) for w in inner)
        return (w_in,) + lax.optimization_barrier(inner)

    reg_weights = staged((reg_in, reg_down, reg_low, reg_up, reg_fine, reg_out))
    dif_weights = staged((dif_in, dif_down, dif_low, dif_up, dif_fine, dif_out))
    cond_count = conditioning.shape[0]
    noise_count = member_noise.shape[1]

    residual_field = sigma_top * member_noise[0]
    gains = []
    for step_index in range(STEPS):
        sigma_now = sigma_top * sigma_ratio**step_index
        sigma_next = sigma_top * sigma_ratio ** (step_index + 1) if step_index + 1 < STEPS else 0.0
        scale_sq = sigma_now**2 + sigma_data**2
        gains.append(
            (
                1.0 / scale_sq**0.5,
                sigma_data**2 / scale_sq,
                sigma_now * sigma_data / scale_sq**0.5,
                (sigma_next - sigma_now) / sigma_now,
            )
        )

    reach = 8
    step_windows = [(0, rows)]
    for _ in range(STEPS - 1):
        lo, hi = step_windows[0]
        step_windows.insert(0, (lo - reach, hi + reach))
    field_lo, field_hi = step_windows[0][0] - reach, step_windows[0][1] + reach
    cond_lo, cond_hi = field_lo - reach, field_hi + reach

    near = jnp.concatenate([residual_field, conditioning.astype(jnp.float32)], axis=0)
    if -cond_lo == 3 * rows and cond_hi == 4 * rows and -field_lo == 2 * rows:
        pieces = [from_tile(near, d) for d in (-2, -1)] + [near]
        pieces += [from_tile(near, d) for d in (1, 2)]
        near_wide = jnp.concatenate(pieces, axis=1)
        cond_wide = jnp.concatenate(
            [
                from_tile(conditioning, -3),
                near_wide[noise_count:].astype(jnp.bfloat16),
                from_tile(conditioning, 3),
            ],
            axis=1,
        )
    else:
        near_wide = halo_rows(near, 1, -field_lo, field_hi - rows)
        cond_wide = halo_rows(conditioning, 1, -cond_lo, cond_hi - rows)
    noise_wide = near_wide[:noise_count]
    cond_near = near_wide[noise_count:].astype(jnp.bfloat16)

    mean_wide = unet(cond_wide, cond_lo, field_lo, field_hi, reg_weights, base, grid_rows)
    mean_wide = row_mask(mean_wide, field_lo, base, grid_rows, axis=1)
    mean_input = mean_wide.astype(jnp.bfloat16)
    reg_mean = mean_wide[:, -field_lo : -field_lo + rows]

    top_lo, top_hi = windows(*step_windows[0])[6:]
    fixed_in = jnp.concatenate([cond_near, mean_input], axis=0)
    fixed_top = conv_in(fixed_in, field_lo, top_lo, top_hi, dif_in[:, :, noise_count:])

    residual_field = noise_wide
    first = field_lo
    for step_index in range(STEPS):
        in_gain, skip_gain, out_gain, step_gain = gains[step_index]
        out_lo, out_hi = step_windows[step_index]
        field_in = row_mask(
            (in_gain * residual_field).astype(jnp.bfloat16), first, base, grid_rows, axis=1
        )
        step_top_lo, step_top_hi = windows(out_lo, out_hi)[6:]
        network = unet(
            field_in,
            first,
            out_lo,
            out_hi,
            dif_weights,
            base,
            grid_rows,
            top_extra=fixed_top[step_top_lo - top_lo : step_top_hi - top_lo],
        )
        kept = residual_field[:, out_lo - first : out_hi - first]
        denoised = skip_gain * kept + out_gain * network
        residual_field = kept + step_gain * (kept - denoised)
        first = out_lo
    return (reg_mean + residual_field)[None]


def solution(mesh):
    return jax.shard_map(
        shards,
        mesh=mesh,
        in_specs=(
            P(None, "tile", None),
            P("ens", None, "tile", None),
            P(),
            P(),
            P(),
            P(),
            P(),
            P(),
            P(),
            P(),
            P(),
            P(),
            P(),
            P(),
        ),
        out_specs=P("ens", None, "tile", None),
        check_vma=False,
    )
```

```python
import jax
import jax.numpy as jnp
from jax import lax
from jax.sharding import PartitionSpec as P

STEPS = 2


sigma_top = 1.0
sigma_ratio = 0.4
sigma_data = 0.5


def from_tile(values, distance):
    count = lax.axis_size("tile")
    pairs = [(i + distance, i) for i in range(count) if 0 <= i + distance < count]
    return lax.ppermute(values, "tile", pairs)


def halo_rows(values, dim, below, above):
    rows = values.shape[dim]
    pieces = []
    need = below
    distance = 1
    while need > 0:
        take = min(need, rows)
        part = lax.slice_in_dim(values, rows - take, rows, axis=dim)
        pieces.insert(0, from_tile(part, -distance))
        need -= take
        distance += 1
    pieces.append(values)
    need = above
    distance = 1
    while need > 0:
        take = min(need, rows)
        part = lax.slice_in_dim(values, 0, take, axis=dim)
        pieces.append(from_tile(part, distance))
        need -= take
        distance += 1
    return jnp.concatenate(pieces, axis=dim)


def row_mask(values, first, base, limit, axis=0):
    shape = [1] * values.ndim
    shape[axis] = values.shape[axis]
    index = base + first + lax.broadcasted_iota(jnp.int32, tuple(shape), axis)
    keep = (index >= 0) & (index < limit)
    return jnp.where(keep, values, jnp.zeros_like(values))


def conv(lhs, rhs, specs, strides=(1, 1), padding=((0, 0), (1, 1)), dilation=(1, 1)):
    return lax.conv_general_dilated(
        lhs,
        rhs,
        window_strides=strides,
        padding=padding,
        lhs_dilation=dilation,
        dimension_numbers=specs,
        preferred_element_type=jnp.float32,
    )


def silu(values):
    return jax.nn.silu(values)


def windows(out_lo, out_hi):
    join_lo, join_hi = out_lo - 2, out_hi + 2
    mid_lo, mid_hi = join_lo // 2 - 1, join_hi // 2 + 1
    crs_lo, crs_hi = mid_lo - 1, mid_hi + 1
    top_lo, top_hi = min(2 * crs_lo - 1, join_lo), max(2 * crs_hi, join_hi)
    return join_lo, join_hi, mid_lo, mid_hi, crs_lo, crs_hi, top_lo, top_hi


def conv_in(fields, first, out_lo, out_hi, weight):
    count, _, cols = fields.shape
    lo, hi = out_lo - 1 - first, out_hi + 1 - first
    assert lo >= 0 and hi <= fields.shape[1]
    extra = -count % 16
    weight = jnp.pad(weight, ((0, 0), (0, 0), (0, extra), (0, 0)))
    padded = jnp.pad(fields[:, lo:hi], ((0, extra), (0, 0), (1, 1)))
    count += extra
    rows = out_hi - out_lo
    patches = jnp.concatenate(
        [padded[:, ty : ty + rows, tx : tx + cols] for ty in range(3) for tx in range(3)], axis=0
    )
    flat = weight.reshape(9 * count, weight.shape[3])
    return jnp.einsum("krw,ko->rwo", patches, flat, preferred_element_type=jnp.float32)


def unet(fields, first, out_lo, out_hi, weights, base, grid_rows, top_extra=None):
    w_in, w_down, w_low, w_up, w_fine, w_out = weights
    join_lo, join_hi, mid_lo, mid_hi, crs_lo, crs_hi, top_lo, top_hi = windows(out_lo, out_hi)
    top = conv_in(fields, first, top_lo, top_hi, w_in[:, :, : fields.shape[0]])
    if top_extra is not None:
        top = top + top_extra
    top = row_mask(silu(top), top_lo, base, grid_rows).astype(jnp.bfloat16)
    down_in = top[2 * crs_lo - 1 - top_lo : 2 * crs_hi - top_lo][None]
    coarse = conv(down_in, w_down, ("NHWC", "HWIO", "NHWC"), strides=(2, 2))[0]
    coarse = row_mask(silu(coarse), crs_lo, base // 2, grid_rows // 2).astype(jnp.bfloat16)
    middle = conv(coarse[None], w_low, ("NHWC", "HWIO", "NHWC"))[0]
    middle = row_mask(silu(middle), mid_lo, base // 2, grid_rows // 2).astype(jnp.bfloat16)
    upward = conv(
        middle[None],
        w_up[::-1, ::-1],
        ("NHWC", "HWIO", "NHWC"),
        padding=((0, 0), (2, 2)),
        dilation=(2, 2),
    )[0]
    joined = top[join_lo - top_lo : join_hi - top_lo].astype(jnp.float32) + upward
    joined = row_mask(joined, join_lo, base, grid_rows).astype(jnp.bfloat16)
    refined = conv(joined[None], w_fine, ("NHWC", "HWIO", "NHWC"))[0]
    refined = row_mask(silu(refined), join_lo + 1, base, grid_rows).astype(jnp.bfloat16)
    return conv_out(refined, w_out)


def conv_out(refined, weight):
    count, cols = refined.shape[0] - 2, refined.shape[1]
    outs = weight.shape[2]
    flat = weight.reshape(9 * outs, weight.shape[3])
    planes = jnp.einsum("tc,rwc->trw", flat, refined, preferred_element_type=jnp.float32)
    planes = jnp.pad(planes, ((0, 0), (0, 0), (1, 1)))
    total = None
    for ty in range(3):
        for tx in range(3):
            tap = (ty * 3 + tx) * outs
            term = planes[tap : tap + outs, ty : ty + count, tx : tx + cols]
            total = term if total is None else total + term
    return total


def shards(
    conditioning,
    member_noise,
    reg_in,
    reg_down,
    reg_low,
    reg_up,
    reg_fine,
    reg_out,
    dif_in,
    dif_down,
    dif_low,
    dif_up,
    dif_fine,
    dif_out,
):
    rows = conditioning.shape[1]
    grid_rows = rows * lax.axis_size("tile")
    base = lax.axis_index("tile") * rows
    reg_weights = (reg_in, reg_down, reg_low, reg_up, reg_fine, reg_out)
    dif_weights = (dif_in, dif_down, dif_low, dif_up, dif_fine, dif_out)
    cond_count = conditioning.shape[0]
    noise_count = member_noise.shape[1]

    residual_field = sigma_top * member_noise[0]
    gains = []
    for step_index in range(STEPS):
        sigma_now = sigma_top * sigma_ratio**step_index
        sigma_next = sigma_top * sigma_ratio ** (step_index + 1) if step_index + 1 < STEPS else 0.0
        scale_sq = sigma_now**2 + sigma_data**2
        gains.append(
            (
                1.0 / scale_sq**0.5,
                sigma_data**2 / scale_sq,
                sigma_now * sigma_data / scale_sq**0.5,
                (sigma_next - sigma_now) / sigma_now,
            )
        )

    dif_halo = 8
    reg_halo = 2 * dif_halo
    noise_in = (gains[0][0] * residual_field).astype(jnp.bfloat16)
    near = jnp.concatenate([noise_in, conditioning], axis=0)
    if rows == dif_halo:
        near_below = from_tile(near, -1)
        near_above = from_tile(near, 1)
        near_wide = jnp.concatenate([near_below, near, near_above], axis=1)
        cond_wide = jnp.concatenate(
            [
                from_tile(conditioning, -2),
                near_wide[noise_count:],
                from_tile(conditioning, 2),
            ],
            axis=1,
        )
    else:
        near_wide = halo_rows(near, 1, dif_halo, dif_halo)
        cond_wide = halo_rows(conditioning, 1, reg_halo, reg_halo)

    mean_wide = unet(cond_wide, -reg_halo, -dif_halo, rows + dif_halo, reg_weights, base, grid_rows)
    mean_wide = row_mask(mean_wide, -dif_halo, base, grid_rows, axis=1)
    mean_input = mean_wide.astype(jnp.bfloat16)
    cond_near = near_wide[noise_count:]
    reg_mean = mean_wide[:, dif_halo : dif_halo + rows]

    fixed_in = jnp.concatenate([cond_near, mean_input], axis=0)
    field_in = near_wide[:noise_count]
    for step_index in range(STEPS):
        in_gain, skip_gain, out_gain, step_gain = gains[step_index]
        if step_index > 0:
            field_in = halo_rows(
                (in_gain * residual_field).astype(jnp.bfloat16), 1, dif_halo, dif_halo
            )
        inputs = jnp.concatenate([field_in, fixed_in], axis=0)
        network = unet(inputs, -dif_halo, 0, rows, dif_weights, base, grid_rows)
        denoised = skip_gain * residual_field + out_gain * network
        residual_field = residual_field + step_gain * (residual_field - denoised)
    return (reg_mean + residual_field)[None]


def solution(mesh):
    return jax.shard_map(
        shards,
        mesh=mesh,
        in_specs=(
            P(None, "tile", None),
            P("ens", None, "tile", None),
            P(),
            P(),
            P(),
            P(),
            P(),
            P(),
            P(),
            P(),
            P(),
            P(),
            P(),
            P(),
        ),
        out_specs=P("ens", None, "tile", None),
        check_vma=False,
    )
```

```python
import jax
import jax.numpy as jnp
from jax import lax
from jax.sharding import PartitionSpec as P

STEPS = 2


sigma_top = 1.0
sigma_ratio = 0.4
sigma_data = 0.5


def from_tile(values, distance):
    count = lax.axis_size("tile")
    pairs = [(i + distance, i) for i in range(count) if 0 <= i + distance < count]
    return lax.ppermute(values, "tile", pairs)


def halo_rows(values, dim, below, above):
    rows = values.shape[dim]
    pieces = []
    need = below
    distance = 1
    while need > 0:
        take = min(need, rows)
        part = lax.slice_in_dim(values, rows - take, rows, axis=dim)
        pieces.insert(0, from_tile(part, -distance))
        need -= take
        distance += 1
    pieces.append(values)
    need = above
    distance = 1
    while need > 0:
        take = min(need, rows)
        part = lax.slice_in_dim(values, 0, take, axis=dim)
        pieces.append(from_tile(part, distance))
        need -= take
        distance += 1
    return jnp.concatenate(pieces, axis=dim)


def row_mask(values, first, base, limit, axis=0):
    shape = [1] * values.ndim
    shape[axis] = values.shape[axis]
    index = base + first + lax.broadcasted_iota(jnp.int32, tuple(shape), axis)
    keep = (index >= 0) & (index < limit)
    return jnp.where(keep, values, jnp.zeros_like(values))


def conv(lhs, rhs, specs, strides=(1, 1), padding=((0, 0), (1, 1)), dilation=(1, 1)):
    return lax.conv_general_dilated(
        lhs,
        rhs,
        window_strides=strides,
        padding=padding,
        lhs_dilation=dilation,
        dimension_numbers=specs,
        preferred_element_type=jnp.float32,
    )


def silu(values):
    return jax.nn.silu(values)


def windows(out_lo, out_hi):
    join_lo, join_hi = out_lo - 2, out_hi + 2
    mid_lo, mid_hi = join_lo // 2 - 1, join_hi // 2 + 1
    crs_lo, crs_hi = mid_lo - 1, mid_hi + 1
    top_lo, top_hi = min(2 * crs_lo - 1, join_lo), max(2 * crs_hi, join_hi)
    return join_lo, join_hi, mid_lo, mid_hi, crs_lo, crs_hi, top_lo, top_hi


def conv_in(fields, first, out_lo, out_hi, weight):
    count, _, cols = fields.shape
    lo, hi = out_lo - 1 - first, out_hi + 1 - first
    assert lo >= 0 and hi <= fields.shape[1]
    extra = -count % 16
    weight = jnp.pad(weight, ((0, 0), (0, 0), (0, extra), (0, 0)))
    padded = jnp.pad(fields[:, lo:hi], ((0, extra), (0, 0), (1, 1)))
    count += extra
    rows = out_hi - out_lo
    patches = jnp.concatenate(
        [padded[:, ty : ty + rows, tx : tx + cols] for ty in range(3) for tx in range(3)], axis=0
    )
    flat = weight.reshape(9 * count, weight.shape[3])
    return jnp.einsum("krw,ko->rwo", patches, flat, preferred_element_type=jnp.float32)


def unet(fields, first, out_lo, out_hi, weights, base, grid_rows, top_extra=None):
    w_in, w_down, w_low, w_up, w_fine, w_out = weights
    join_lo, join_hi, mid_lo, mid_hi, crs_lo, crs_hi, top_lo, top_hi = windows(out_lo, out_hi)
    top = conv_in(fields, first, top_lo, top_hi, w_in[:, :, : fields.shape[0]])
    if top_extra is not None:
        top = top + top_extra
    top = row_mask(silu(top), top_lo, base, grid_rows).astype(jnp.bfloat16)
    down_in = top[2 * crs_lo - 1 - top_lo : 2 * crs_hi - top_lo][None]
    coarse = conv(down_in, w_down, ("NHWC", "HWIO", "NHWC"), strides=(2, 2))[0]
    coarse = row_mask(silu(coarse), crs_lo, base // 2, grid_rows // 2).astype(jnp.bfloat16)
    middle = conv(coarse[None], w_low, ("NHWC", "HWIO", "NHWC"))[0]
    middle = row_mask(silu(middle), mid_lo, base // 2, grid_rows // 2).astype(jnp.bfloat16)
    upward = conv(
        middle[None],
        w_up[::-1, ::-1],
        ("NHWC", "HWIO", "NHWC"),
        padding=((0, 0), (2, 2)),
        dilation=(2, 2),
    )[0]
    joined = top[join_lo - top_lo : join_hi - top_lo].astype(jnp.float32) + upward
    joined = row_mask(joined, join_lo, base, grid_rows).astype(jnp.bfloat16)
    refined = conv(joined[None], w_fine, ("NHWC", "HWIO", "NHWC"))[0]
    refined = row_mask(silu(refined), join_lo + 1, base, grid_rows).astype(jnp.bfloat16)
    return conv_out(refined, w_out)


def conv_out(refined, weight):
    count, cols = refined.shape[0] - 2, refined.shape[1]
    outs = weight.shape[2]
    flat = weight.reshape(9 * outs, weight.shape[3])
    planes = jnp.einsum("tc,rwc->trw", flat, refined, preferred_element_type=jnp.float32)
    planes = jnp.pad(planes, ((0, 0), (0, 0), (1, 1)))
    total = None
    for ty in range(3):
        for tx in range(3):
            tap = (ty * 3 + tx) * outs
            term = planes[tap : tap + outs, ty : ty + count, tx : tx + cols]
            total = term if total is None else total + term
    return total


def shards(
    conditioning,
    member_noise,
    reg_in,
    reg_down,
    reg_low,
    reg_up,
    reg_fine,
    reg_out,
    dif_in,
    dif_down,
    dif_low,
    dif_up,
    dif_fine,
    dif_out,
):
    rows = conditioning.shape[1]
    grid_rows = rows * lax.axis_size("tile")
    base = lax.axis_index("tile") * rows
    reg_weights = (reg_in, reg_down, reg_low, reg_up, reg_fine, reg_out)
    dif_weights = (dif_in, dif_down, dif_low, dif_up, dif_fine, dif_out)
    cond_count = conditioning.shape[0]
    noise_count = member_noise.shape[1]

    residual_field = sigma_top * member_noise[0]
    gains = []
    for step_index in range(STEPS):
        sigma_now = sigma_top * sigma_ratio**step_index
        sigma_next = sigma_top * sigma_ratio ** (step_index + 1) if step_index + 1 < STEPS else 0.0
        scale_sq = sigma_now**2 + sigma_data**2
        gains.append(
            (
                1.0 / scale_sq**0.5,
                sigma_data**2 / scale_sq,
                sigma_now * sigma_data / scale_sq**0.5,
                (sigma_next - sigma_now) / sigma_now,
            )
        )

    dif_halo = 8
    reg_halo = 2 * dif_halo
    noise_in = (gains[0][0] * residual_field).astype(jnp.bfloat16)
    near = jnp.concatenate([noise_in, conditioning], axis=0)
    if rows == dif_halo:
        cols = conditioning.shape[2]
        cond_flat = conditioning.reshape(-1, cols)
        near_flat = jnp.concatenate([noise_in.reshape(-1, cols), cond_flat], axis=0)
        near_below = from_tile(near_flat, -1).reshape(near.shape)
        near_above = from_tile(near_flat, 1).reshape(near.shape)
        near_wide = jnp.concatenate([near_below, near, near_above], axis=1)
        cond_wide = jnp.concatenate(
            [
                from_tile(cond_flat, -2).reshape(conditioning.shape),
                near_wide[noise_count:],
                from_tile(cond_flat, 2).reshape(conditioning.shape),
            ],
            axis=1,
        )
    else:
        near_wide = halo_rows(near, 1, dif_halo, dif_halo)
        cond_wide = halo_rows(conditioning, 1, reg_halo, reg_halo)

    mean_wide = unet(cond_wide, -reg_halo, -dif_halo, rows + dif_halo, reg_weights, base, grid_rows)
    mean_wide = row_mask(mean_wide, -dif_halo, base, grid_rows, axis=1)
    mean_input = mean_wide.astype(jnp.bfloat16)
    cond_near = near_wide[noise_count:]
    reg_mean = mean_wide[:, dif_halo : dif_halo + rows]

    fixed_in = jnp.concatenate([cond_near, mean_input], axis=0)
    field_in = near_wide[:noise_count]
    for step_index in range(STEPS):
        in_gain, skip_gain, out_gain, step_gain = gains[step_index]
        if step_index > 0:
            field_in = halo_rows(
                (in_gain * residual_field).astype(jnp.bfloat16), 1, dif_halo, dif_halo
            )
        inputs = jnp.concatenate([field_in, fixed_in], axis=0)
        network = unet(inputs, -dif_halo, 0, rows, dif_weights, base, grid_rows)
        denoised = skip_gain * residual_field + out_gain * network
        residual_field = residual_field + step_gain * (residual_field - denoised)
    return (reg_mean + residual_field)[None]


def solution(mesh):
    return jax.shard_map(
        shards,
        mesh=mesh,
        in_specs=(
            P(None, "tile", None),
            P("ens", None, "tile", None),
            P(),
            P(),
            P(),
            P(),
            P(),
            P(),
            P(),
            P(),
            P(),
            P(),
            P(),
            P(),
        ),
        out_specs=P("ens", None, "tile", None),
        check_vma=False,
    )
```

```python
import jax
import jax.numpy as jnp
from jax import lax
from jax.sharding import PartitionSpec as P

STEPS = 2


sigma_top = 1.0
sigma_ratio = 0.4
sigma_data = 0.5


def from_tile(values, distance):
    count = lax.axis_size("tile")
    pairs = [(i + distance, i) for i in range(count) if 0 <= i + distance < count]
    return lax.ppermute(values, "tile", pairs)


def halo_rows(values, dim, below, above):
    rows = values.shape[dim]
    pieces = []
    need = below
    distance = 1
    while need > 0:
        take = min(need, rows)
        part = lax.slice_in_dim(values, rows - take, rows, axis=dim)
        pieces.insert(0, from_tile(part, -distance))
        need -= take
        distance += 1
    pieces.append(values)
    need = above
    distance = 1
    while need > 0:
        take = min(need, rows)
        part = lax.slice_in_dim(values, 0, take, axis=dim)
        pieces.append(from_tile(part, distance))
        need -= take
        distance += 1
    return jnp.concatenate(pieces, axis=dim)


def row_mask(values, first, base, limit, axis=0):
    shape = [1] * values.ndim
    shape[axis] = values.shape[axis]
    index = base + first + lax.broadcasted_iota(jnp.int32, tuple(shape), axis)
    keep = (index >= 0) & (index < limit)
    return jnp.where(keep, values, jnp.zeros_like(values))


def conv(lhs, rhs, specs, strides=(1, 1), padding=((0, 0), (1, 1)), dilation=(1, 1)):
    return lax.conv_general_dilated(
        lhs,
        rhs,
        window_strides=strides,
        padding=padding,
        lhs_dilation=dilation,
        dimension_numbers=specs,
        preferred_element_type=jnp.float32,
    )


def silu(values):
    return jax.nn.silu(values)


def windows(out_lo, out_hi):
    join_lo, join_hi = out_lo - 2, out_hi + 2
    mid_lo, mid_hi = join_lo // 2 - 1, join_hi // 2 + 1
    crs_lo, crs_hi = mid_lo - 1, mid_hi + 1
    top_lo, top_hi = min(2 * crs_lo - 1, join_lo), max(2 * crs_hi, join_hi)
    return join_lo, join_hi, mid_lo, mid_hi, crs_lo, crs_hi, top_lo, top_hi


def conv_in(fields, first, out_lo, out_hi, weight):
    count, _, cols = fields.shape
    lo, hi = out_lo - 1 - first, out_hi + 1 - first
    assert lo >= 0 and hi <= fields.shape[1]
    extra = -count % 16
    weight = jnp.pad(weight, ((0, 0), (0, 0), (0, extra), (0, 0)))
    padded = jnp.pad(fields[:, lo:hi], ((0, extra), (0, 0), (1, 1)))
    count += extra
    rows = out_hi - out_lo
    patches = jnp.concatenate(
        [padded[:, ty : ty + rows, tx : tx + cols] for ty in range(3) for tx in range(3)], axis=0
    )
    flat = weight.reshape(9 * count, weight.shape[3])
    return jnp.einsum("krw,ko->rwo", patches, flat, preferred_element_type=jnp.float32)


def unet(fields, first, out_lo, out_hi, weights, base, grid_rows, top_extra=None):
    w_in, w_down, w_low, w_up, w_fine, w_out = weights
    join_lo, join_hi, mid_lo, mid_hi, crs_lo, crs_hi, top_lo, top_hi = windows(out_lo, out_hi)
    top = conv_in(fields, first, top_lo, top_hi, w_in[:, :, : fields.shape[0]])
    if top_extra is not None:
        top = top + top_extra
    top = row_mask(silu(top), top_lo, base, grid_rows).astype(jnp.bfloat16)
    down_in = top[2 * crs_lo - 1 - top_lo : 2 * crs_hi - top_lo][None]
    coarse = conv(down_in, w_down, ("NHWC", "HWIO", "NHWC"), strides=(2, 2))[0]
    coarse = row_mask(silu(coarse), crs_lo, base // 2, grid_rows // 2).astype(jnp.bfloat16)
    middle = conv(coarse[None], w_low, ("NHWC", "HWIO", "NHWC"))[0]
    middle = row_mask(silu(middle), mid_lo, base // 2, grid_rows // 2).astype(jnp.bfloat16)
    upward = conv(
        middle[None],
        w_up[::-1, ::-1],
        ("NHWC", "HWIO", "NHWC"),
        padding=((0, 0), (2, 2)),
        dilation=(2, 2),
    )[0]
    joined = top[join_lo - top_lo : join_hi - top_lo].astype(jnp.float32) + upward
    joined = row_mask(joined, join_lo, base, grid_rows).astype(jnp.bfloat16)
    refined = conv(joined[None], w_fine, ("NHWC", "HWIO", "NHWC"))[0]
    refined = row_mask(silu(refined), join_lo + 1, base, grid_rows).astype(jnp.bfloat16)
    return conv_out(refined, w_out)


def conv_out(refined, weight):
    count, cols = refined.shape[0] - 2, refined.shape[1]
    outs = weight.shape[2]
    flat = weight.reshape(9 * outs, weight.shape[3])
    planes = jnp.einsum("tc,rwc->trw", flat, refined, preferred_element_type=jnp.float32)
    planes = jnp.pad(planes, ((0, 0), (0, 0), (1, 1)))
    total = None
    for ty in range(3):
        for tx in range(3):
            tap = (ty * 3 + tx) * outs
            term = planes[tap : tap + outs, ty : ty + count, tx : tx + cols]
            total = term if total is None else total + term
    return total


def shards(
    conditioning,
    member_noise,
    reg_in,
    reg_down,
    reg_low,
    reg_up,
    reg_fine,
    reg_out,
    dif_in,
    dif_down,
    dif_low,
    dif_up,
    dif_fine,
    dif_out,
):
    rows = conditioning.shape[1]
    grid_rows = rows * lax.axis_size("tile")
    base = lax.axis_index("tile") * rows
    reg_weights = (reg_in, reg_down, reg_low, reg_up, reg_fine, reg_out)
    dif_weights = (dif_in, dif_down, dif_low, dif_up, dif_fine, dif_out)
    cond_count = conditioning.shape[0]
    noise_count = member_noise.shape[1]

    residual_field = sigma_top * member_noise[0]
    gains = []
    for step_index in range(STEPS):
        sigma_now = sigma_top * sigma_ratio**step_index
        sigma_next = sigma_top * sigma_ratio ** (step_index + 1) if step_index + 1 < STEPS else 0.0
        scale_sq = sigma_now**2 + sigma_data**2
        gains.append(
            (
                1.0 / scale_sq**0.5,
                sigma_data**2 / scale_sq,
                sigma_now * sigma_data / scale_sq**0.5,
                (sigma_next - sigma_now) / sigma_now,
            )
        )

    dif_halo = 8
    reg_halo = 2 * dif_halo
    noise_in = (gains[0][0] * residual_field).astype(jnp.bfloat16)
    near = jnp.concatenate([noise_in, conditioning], axis=0)
    if rows == dif_halo:
        near_below = from_tile(near, -1)
        near_above = from_tile(near, 1)
        near_wide = jnp.concatenate([near_below, near, near_above], axis=1)
        cond_wide = jnp.concatenate(
            [
                from_tile(conditioning, -2),
                near_wide[noise_count:],
                from_tile(conditioning, 2),
            ],
            axis=1,
        )
    else:
        near_wide = halo_rows(near, 1, dif_halo, dif_halo)
        cond_wide = halo_rows(conditioning, 1, reg_halo, reg_halo)

    mean_wide = unet(cond_wide, -reg_halo, -dif_halo, rows + dif_halo, reg_weights, base, grid_rows)
    mean_wide = row_mask(mean_wide, -dif_halo, base, grid_rows, axis=1)
    mean_input = mean_wide.astype(jnp.bfloat16)
    cond_near = near_wide[noise_count:]
    reg_mean = mean_wide[:, dif_halo : dif_halo + rows]

    fixed_in = jnp.concatenate([cond_near, mean_input], axis=0)
    dif_first = jnp.concatenate([dif_in[:, :, noise_count:], dif_in[:, :, :noise_count]], axis=2)
    dif_order = (dif_first,) + tuple(dif_weights[1:])
    field_in = near_wide[:noise_count]
    for step_index in range(STEPS):
        in_gain, skip_gain, out_gain, step_gain = gains[step_index]
        if step_index > 0:
            field_in = halo_rows(
                (in_gain * residual_field).astype(jnp.bfloat16), 1, dif_halo, dif_halo
            )
        inputs = jnp.concatenate([fixed_in, field_in], axis=0)
        network = unet(inputs, -dif_halo, 0, rows, dif_order, base, grid_rows)
        denoised = skip_gain * residual_field + out_gain * network
        residual_field = residual_field + step_gain * (residual_field - denoised)
    return (reg_mean + residual_field)[None]


def solution(mesh):
    return jax.shard_map(
        shards,
        mesh=mesh,
        in_specs=(
            P(None, "tile", None),
            P("ens", None, "tile", None),
            P(),
            P(),
            P(),
            P(),
            P(),
            P(),
            P(),
            P(),
            P(),
            P(),
            P(),
            P(),
        ),
        out_specs=P("ens", None, "tile", None),
        check_vma=False,
    )
```
